32 devices in a mesh: grp: 8 (over y, x, core), rep: 4 (over z).
Axes of the slice: x: 2, y: 2, z: 4, core: 2. Of those that a mesh axis runs over, the one named last changes fastest.
Arguments:
- features: bfloat16 [4096, 256], P(('grp', 'rep')), may hold values from -0.0625 to 0.0625
- weight: bfloat16 [256, 256], replicated, may hold values from -0.375 to 0.375
- preact: bfloat16 [4096, 256], P(('grp', 'rep')), may hold values from -6 to 6
- grad_out: bfloat16 [4096, 256], P(('grp', 'rep')), may hold values from -1.5 to 1.5
- degree: int32 [4096], P(('grp', 'rep')), may hold values from 1 to 64
- tile_values: bfloat16 [256, 4, 128, 128], P(('grp', 'rep')), may hold values from 0 to 1
- tile_rows: int32 [256, 4], P(('grp', 'rep')), may hold values from -1 to 3, as said below
Outputs:
- input_grad: float32 [4096, 256], P(('grp', 'rep'))
- weight_grad: float32 [256, 256], replicated
The draws below stay inside these ranges and needn't reach their ends.
Inputs may be any that keep to these rules, and one draw needn't show every extreme that they name: `tile_rows`: each of the 8 rows of one device (aligned blocks) has up to 4 live slots; in every such block some row has all 4 slots live.
All inputs are finite; a program needn't handle non-finite values.
Results may differ from the reference program's by a relative error of at most 0.013.
Values may be sent and summed in bfloat16 or wider, within the bound.
No kernel may reach another device: no remote copies, remote signals or barrier semaphores. Data moves between devices by JAX's collectives and lax.ppermute only.
A program may use at most 128 MiB of HBM per device.

```python
import jax
import jax.numpy as jnp
from jax import lax

F = 256
TILE = 128
SLOTS = 4
ROWS_DEV = 128
BLOCK_ROWS = 512
NODES = 4096
TILE_COLS = 8
ROW_TILES = 4
ALL_COLS = 256
N_GRP = 8
N_REP = 4


def draw_tile_rows(key, part):
    key_rows, key_dense, key_coins, key_full = jax.random.split(key, 4)
    owners = ALL_COLS // TILE_COLS
    row_ids = jax.random.randint(key_rows, (owners, TILE_COLS, SLOTS), 0, ROW_TILES)
    density = jax.random.randint(key_dense, (owners, 1, 1), 1, 4)
    coins = jax.random.randint(key_coins, (owners, TILE_COLS, SLOTS), 0, 4)
    chosen = jax.random.randint(key_full, (owners, 1, 1), 0, TILE_COLS)
    column = lax.broadcasted_iota(jnp.int32, (owners, TILE_COLS, SLOTS), 1)
    tile_live = (coins < density) | (column == chosen)
    return jnp.where(tile_live, row_ids, -1).reshape(ALL_COLS, SLOTS).astype(jnp.int32)


def plant(drawn, own_key, smallest, largest):
    shape = drawn.shape
    place = [jax.random.randint(jax.random.fold_in(own_key, axis), (), 0, shape[axis]) for axis in range(len(shape))]
    drawn = drawn.at[tuple(place)].set(smallest)
    longest = shape.index(max(shape))
    place[longest] = (place[longest] + 1) % shape[longest]
    return drawn.at[tuple(place)].set(largest)


def shard_levels(key, shape, cuts, least, high):
    factor_of, own = 1.0, jax.random.fold_in(key, 6)
    for position, blocks in cuts:
        draws = jnp.exp(jax.random.uniform(jax.random.fold_in(own, position), (blocks,), jnp.float32, least / len(cuts), high / len(cuts)))
        factor_of = factor_of * jnp.repeat(draws, shape[position] // blocks).reshape([-1 if axis == position else 1 for axis in range(len(shape))])
    return factor_of


def gaussian(own_key, dims, width, most, pieces=(), kind=jnp.bfloat16):
    values = width * jax.random.normal(own_key, dims, jnp.float32)
    if pieces:
        values = values * shard_levels(own_key, dims, pieces, -0.22, 0.18)
    return jnp.clip(values, -most, most).astype(kind)


def setup_inputs(seed: int = 0) -> dict:
    arg_keys = jax.random.split(jax.random.key(seed), 8)
    return {
        "features": gaussian(arg_keys[0], (NODES, F), 0.01, 0.0625, ((0, 32),)),
        "weight": gaussian(arg_keys[1], (F, F), F ** -0.5, 0.375),
        "preact": gaussian(arg_keys[2], (NODES, F), 1.0, 6.0, ((0, 32),)),
        "grad_out": gaussian(arg_keys[3], (NODES, F), 0.25, 1.5, ((0, 32),)),
        "degree": plant(jax.random.randint(arg_keys[4], (NODES,), 1, 65), jax.random.fold_in(arg_keys[4], 1), 1, 64).astype(jnp.int32),
        "tile_values": jnp.clip(1.0 * jax.random.uniform(arg_keys[5], (ALL_COLS, SLOTS, TILE, TILE), jnp.float32) ** shard_levels(arg_keys[5], (ALL_COLS, SLOTS, TILE, TILE), ((0, 32),), -0.2, 0.2), 0.0, 1.0).astype(jnp.bfloat16),
        "tile_rows": draw_tile_rows(jax.random.fold_in(arg_keys[7], 71), 0),
    }


def reference(features, weight, preact, grad_out, degree, tile_values, tile_rows):
    highest = lax.Precision.HIGHEST
    scaling = lax.rsqrt(degree.astype(jnp.float32))[:, None]
    grad_pre = jnp.where(preact > 0, grad_out, jnp.zeros_like(grad_out))
    scaled = (features.astype(jnp.float32) * scaling).astype(jnp.bfloat16)
    projected = (scaling * lax.dot_general(grad_pre, weight, (((1,), (1,)), ((), ())), preferred_element_type=jnp.float32)).astype(jnp.bfloat16)
    per_block = ROWS_DEV // TILE
    col_feats = scaled.reshape(N_GRP, N_REP, per_block, TILE, F)
    row_range = jnp.arange(ROW_TILES, dtype=jnp.int32)

    def per_row_block(totals, block_id):
        values_all = lax.dynamic_slice_in_dim(tile_values, (block_id * N_REP * TILE_COLS).astype(jnp.int32), N_REP * TILE_COLS, 0)
        values_all = values_all.reshape(N_REP, TILE_COLS, SLOTS, TILE, TILE)
        row_ids = lax.dynamic_slice_in_dim(tile_rows, (block_id * N_REP * TILE_COLS).astype(jnp.int32), N_REP * TILE_COLS, 0)
        row_ids = row_ids.reshape(N_REP, TILE_COLS, SLOTS)
        block_rows = lax.dynamic_slice_in_dim(projected, (block_id * BLOCK_ROWS).astype(jnp.int32), BLOCK_ROWS, 0)
        block_rows = block_rows.reshape(ROW_TILES, TILE, F).astype(jnp.float32)
        summed = jnp.zeros((ROW_TILES, TILE, F), jnp.float32)
        returned = []
        for replica in range(N_REP):
            tile_live = row_ids[replica] >= 0
            clipped = jnp.where(tile_live, row_ids[replica], 0)
            onehot = ((clipped[..., None] == row_range) & tile_live[..., None]).astype(jnp.float32)
            values_f = values_all[replica].astype(jnp.float32)
            columns = col_feats[:, replica].reshape(TILE_COLS, TILE, F).astype(jnp.float32)
            product = jnp.einsum('csij,cjf->csif', values_f, columns, precision=highest)
            summed = summed + jnp.einsum('csr,csif->rif', onehot, product, precision=highest)
            picked = jnp.einsum('csr,rif->csif', onehot, block_rows, precision=highest)
            returned.append(jnp.einsum('csij,csif->cjf', values_f, picked, precision=highest))
        return (totals + jnp.stack(returned), summed.reshape(BLOCK_ROWS, F))
    start_totals = jnp.zeros((N_REP, TILE_COLS, TILE, F), jnp.float32)
    totals, gathered = lax.scan(per_row_block, start_totals, jnp.arange(N_GRP, dtype=jnp.int32))
    aggregated = (scaling * gathered.reshape(NODES, F)).astype(jnp.bfloat16)
    weight_grad = lax.dot_general(aggregated, grad_pre, (((0,), (0,)), ((), ())), preferred_element_type=jnp.float32)
    transposed = totals.reshape(N_REP, N_GRP, per_block, TILE, F).transpose(1, 0, 2, 3, 4).reshape(NODES, F)
    input_grad = scaling * transposed
    return (input_grad, weight_grad)
```

```python
import jax
import jax.numpy as jnp
from jax import lax
from jax.sharding import PartitionSpec as P

HIGHEST = lax.Precision.HIGHEST


def gather_rep(x):
    reps = lax.axis_size("rep")
    me = lax.axis_index("rep")
    parts = [x]
    for shift in range(1, reps):
        parts.append(lax.ppermute(x, "rep", [((i + shift) % reps, i) for i in range(reps)]))
    stacked = jnp.stack(parts)
    return jnp.roll(stacked, me, axis=0)


def all_reduce_a2a(w, axes):
    count = 1
    for name in axes:
        count *= lax.axis_size(name)
    chunks = w.reshape(count, -1)
    owned = lax.all_to_all(chunks, axes, 0, 0, tiled=True).reshape(count, -1).sum(0)
    spread = jnp.broadcast_to(owned[None], (count, owned.shape[0]))
    return lax.all_to_all(spread, axes, 0, 0, tiled=True).reshape(w.shape)


def per_device(features, weight, preact, grad_out, degree, tile_values, tile_rows):
    rows_here, width = features.shape
    col_tiles, slots, edge, _ = tile_values.shape
    reps = lax.axis_size("rep")
    row_tiles = reps * rows_here // edge
    inverse = lax.rsqrt(degree.astype(jnp.float32))[:, None]
    grad_pre = jnp.where(preact > 0, grad_out, jnp.zeros_like(grad_out))
    scaled = (features.astype(jnp.float32) * inverse).astype(jnp.bfloat16)
    projected = (
        lax.dot_general(
            grad_pre, weight, (((1,), (1,)), ((), ())), preferred_element_type=jnp.float32
        )
        * inverse
    ).astype(jnp.bfloat16)

    columns = lax.all_gather(scaled, "grp", axis=0, tiled=True).reshape(col_tiles, edge, width)
    degree_lanes = jnp.broadcast_to(degree.astype(jnp.bfloat16)[:, None], (rows_here, 128))
    packed = jnp.concatenate([projected, grad_pre, degree_lanes], axis=1)
    block = gather_rep(packed).reshape(reps * rows_here, -1)
    block_proj = block[:, :width].reshape(row_tiles, edge, width)
    block_grad = block[:, width : 2 * width].astype(jnp.float32)
    block_inverse = lax.rsqrt(block[:, 2 * width : 2 * width + 1].astype(jnp.float32))

    tile_live = tile_rows >= 0
    clipped = jnp.where(tile_live, tile_rows, 0)
    onehot = (
        (clipped[..., None] == jnp.arange(row_tiles, dtype=jnp.int32)) & tile_live[..., None]
    ).astype(jnp.float32)

    product = jnp.einsum(
        "csij,cjf->csif", tile_values, columns, preferred_element_type=jnp.float32
    )
    partial = jnp.einsum("csh,csif->hif", onehot, product, precision=HIGHEST)
    partial = partial.reshape(row_tiles * edge, width) * block_inverse
    weight_local = lax.dot_general(
        partial, block_grad, (((0,), (0,)), ((), ())), precision=HIGHEST,
        preferred_element_type=jnp.float32,
    )

    picked = jnp.take(block_proj, clipped, axis=0)
    picked = jnp.where(tile_live[:, :, None, None], picked, jnp.zeros_like(picked))
    result = jnp.einsum("csij,csif->cjf", tile_values, picked, preferred_element_type=jnp.float32)

    terms = lax.all_to_all(result, "grp", 0, 0, tiled=True)
    input_grad = terms.sum(0) * inverse
    weight_grad = all_reduce_a2a(weight_local, ("grp", "rep"))
    return (input_grad, weight_grad)


def solution(mesh):
    return jax.shard_map(
        per_device,
        mesh=mesh,
        in_specs=(
            P(("grp", "rep"), None),
            P(),
            P(("grp", "rep"), None),
            P(("grp", "rep"), None),
            P(("grp", "rep")),
            P(("grp", "rep"), None, None, None),
            P(("grp", "rep"), None),
        ),
        out_specs=(P(("grp", "rep"), None), P()),
        check_vma=False,
    )
```

```python
import jax
import jax.numpy as jnp
from jax import lax
from jax.sharding import PartitionSpec as P

HIGHEST = lax.Precision.HIGHEST


def all_reduce_a2a(w, axes):
    count = 1
    for name in axes:
        count *= lax.axis_size(name)
    chunks = w.reshape(count, -1)
    owned = lax.all_to_all(chunks, axes, 0, 0, tiled=True).reshape(count, -1).sum(0)
    spread = jnp.broadcast_to(owned[None], (count, owned.shape[0]))
    return lax.all_to_all(spread, axes, 0, 0, tiled=True).reshape(w.shape)


def gather_axis(x, axis):
    count = lax.axis_size(axis)
    me = lax.axis_index(axis)
    parts = [x]
    for shift in range(1, count):
        parts.append(lax.ppermute(x, axis, [((i + shift) % count, i) for i in range(count)]))
    stacked = jnp.stack(parts)
    return jnp.roll(stacked, me, axis=0)


def per_device(features, weight, preact, grad_out, degree, tile_values, tile_rows):
    rows_here, width = features.shape
    col_tiles, slots, edge, _ = tile_values.shape
    reps = lax.axis_size("rep")
    row_tiles = reps * rows_here // edge
    inverse = lax.rsqrt(degree.astype(jnp.float32))[:, None]
    grad_pre = jnp.where(preact > 0, grad_out, jnp.zeros_like(grad_out))
    scaled = (features.astype(jnp.float32) * inverse).astype(jnp.bfloat16)

    columns = gather_axis(scaled, "grp").reshape(col_tiles, edge, width)
    degree_row = jnp.zeros((16, width), jnp.bfloat16).at[0, :rows_here].set(
        degree.astype(jnp.bfloat16)
    )
    packed = jnp.concatenate([grad_pre, degree_row], axis=0)
    block = gather_axis(packed, "rep")
    block_grad = block[:, :rows_here].reshape(reps * rows_here, width)
    block_degree = block[:, rows_here, :rows_here].reshape(reps * rows_here, 1)
    block_inverse = lax.rsqrt(block_degree.astype(jnp.float32))
    block_proj = (
        lax.dot_general(
            block_grad, weight, (((1,), (1,)), ((), ())), preferred_element_type=jnp.float32
        )
        * block_inverse
    ).astype(jnp.bfloat16).reshape(row_tiles, edge, width)

    hit = tile_rows[None] == jnp.arange(row_tiles, dtype=jnp.int32)[:, None, None]
    masked = jnp.where(hit[..., None, None], tile_values[None], jnp.zeros_like(tile_values[None]))

    partial = jnp.einsum("hcsij,cjf->hif", masked, columns, preferred_element_type=jnp.float32)
    partial = partial.reshape(row_tiles * edge, width) * block_inverse
    weight_local = lax.dot_general(
        partial, block_grad.astype(jnp.float32), (((0,), (0,)), ((), ())), precision=HIGHEST,
        preferred_element_type=jnp.float32,
    )

    result = jnp.einsum("hcsij,hif->cjf", masked, block_proj, preferred_element_type=jnp.float32)

    terms = lax.all_to_all(result.astype(jnp.bfloat16), "grp", 0, 0, tiled=True)
    input_grad = terms.astype(jnp.float32).sum(0) * inverse
    weight_grad = all_reduce_a2a(weight_local, ("grp", "rep"))
    return (input_grad, weight_grad)


def solution(mesh):
    return jax.shard_map(
        per_device,
        mesh=mesh,
        in_specs=(
            P(("grp", "rep"), None),
            P(),
            P(("grp", "rep"), None),
            P(("grp", "rep"), None),
            P(("grp", "rep")),
            P(("grp", "rep"), None, None, None),
            P(("grp", "rep"), None),
        ),
        out_specs=(P(("grp", "rep"), None), P()),
        check_vma=False,
    )
```

```python
import jax
import jax.numpy as jnp
from jax import lax
from jax.sharding import PartitionSpec as P

HIGHEST = lax.Precision.HIGHEST


def all_reduce_a2a(w, axes):
    count = 1
    for name in axes:
        count *= lax.axis_size(name)
    chunks = w.reshape(count, -1)
    owned = lax.all_to_all(chunks, axes, 0, 0, tiled=True).reshape(count, -1).sum(0)
    spread = jnp.broadcast_to(owned[None], (count, owned.shape[0]))
    return lax.all_to_all(spread, axes, 0, 0, tiled=True).reshape(w.shape)


def per_device(features, weight, preact, grad_out, degree, tile_values, tile_rows):
    rows_here, width = features.shape
    col_tiles, slots, edge, _ = tile_values.shape
    reps = lax.axis_size("rep")
    row_tiles = reps * rows_here // edge
    inverse = lax.rsqrt(degree.astype(jnp.float32))[:, None]
    grad_pre = jnp.where(preact > 0, grad_out, jnp.zeros_like(grad_out))
    scaled = (features.astype(jnp.float32) * inverse).astype(jnp.bfloat16)

    degree_row = jnp.zeros((16, width), jnp.bfloat16).at[0, :rows_here].set(
        degree.astype(jnp.bfloat16)
    )
    packed = jnp.concatenate([grad_pre, degree_row], axis=0)
    block = lax.all_gather(packed, "rep", axis=0, tiled=False)
    block_grad = block[:, :rows_here].reshape(reps * rows_here, width)
    block_degree = block[:, rows_here, :rows_here].reshape(reps * rows_here, 1)
    block_inverse = lax.rsqrt(block_degree.astype(jnp.float32))
    block_scaled_grad = (block_grad.astype(jnp.float32) * block_inverse).astype(jnp.bfloat16)
    block_scaled_grad = block_scaled_grad.reshape(row_tiles, edge, width)

    hit = tile_rows[None] == jnp.arange(row_tiles, dtype=jnp.int32)[:, None, None]
    masked = jnp.where(hit[..., None, None], tile_values[None], jnp.zeros_like(tile_values[None]))
    terms = jnp.einsum(
        "hcsij,hif->cjf", masked, block_scaled_grad, preferred_element_type=jnp.float32
    )

    arrived = lax.all_to_all(terms.astype(jnp.bfloat16), "grp", 0, 0, tiled=True)
    pulled = arrived.astype(jnp.float32).sum(0)

    input_grad = inverse * lax.dot_general(
        pulled, weight.astype(jnp.float32), (((1,), (1,)), ((), ())), precision=HIGHEST,
        preferred_element_type=jnp.float32,
    )
    weight_local = lax.dot_general(
        scaled.astype(jnp.float32), pulled, (((0,), (0,)), ((), ())), precision=HIGHEST,
        preferred_element_type=jnp.float32,
    )
    weight_grad = all_reduce_a2a(weight_local, ("grp", "rep"))
    return (input_grad, weight_grad)


def solution(mesh):
    return jax.shard_map(
        per_device,
        mesh=mesh,
        in_specs=(
            P(("grp", "rep"), None),
            P(),
            P(("grp", "rep"), None),
            P(("grp", "rep"), None),
            P(("grp", "rep")),
            P(("grp", "rep"), None, None, None),
            P(("grp", "rep"), None),
        ),
        out_specs=(P(("grp", "rep"), None), P()),
        check_vma=False,
    )
```

```python
import jax
import jax.numpy as jnp
from jax import lax
from jax.sharding import PartitionSpec as P

HIGHEST = lax.Precision.HIGHEST


def all_reduce_a2a(w, axes):
    count = 1
    for name in axes:
        count *= lax.axis_size(name)
    chunks = w.reshape(count, -1)
    owned = lax.all_to_all(chunks, axes, 0, 0, tiled=True).reshape(count, -1).sum(0)
    spread = jnp.broadcast_to(owned[None], (count, owned.shape[0]))
    return lax.all_to_all(spread, axes, 0, 0, tiled=True).reshape(w.shape)


def per_device(features, weight, preact, grad_out, degree, tile_values, tile_rows):
    rows_here, width = features.shape
    col_tiles, slots, edge, _ = tile_values.shape
    reps = lax.axis_size("rep")
    row_tiles = reps * rows_here // edge
    inverse = lax.rsqrt(degree.astype(jnp.float32))[:, None]
    grad_pre = jnp.where(preact > 0, grad_out, jnp.zeros_like(grad_out))
    scaled = (features.astype(jnp.float32) * inverse).astype(jnp.bfloat16)

    degree_row = jnp.zeros((16, width), jnp.bfloat16).at[0, :rows_here].set(
        degree.astype(jnp.bfloat16)
    )
    packed = jnp.concatenate([grad_pre, degree_row], axis=0)
    me = lax.axis_index("rep")
    parts = [packed]
    for shift in range(1, reps):
        parts.append(lax.ppermute(packed, "rep", [((i + shift) % reps, i) for i in range(reps)]))
    block = jnp.stack(parts)
    block_grad = block[:, :rows_here].reshape(reps * rows_here, width)
    block_degree = block[:, rows_here, :rows_here].reshape(reps * rows_here, 1)
    block_inverse = lax.rsqrt(block_degree.astype(jnp.float32))
    block_scaled_grad = (block_grad.astype(jnp.float32) * block_inverse).astype(jnp.bfloat16)
    block_scaled_grad = block_scaled_grad.reshape(row_tiles, edge, width)

    arrival = jnp.where(tile_rows >= 0, (tile_rows - me + reps) % reps, -1)
    hit = arrival[None] == jnp.arange(row_tiles, dtype=jnp.int32)[:, None, None]
    masked = jnp.where(hit[..., None, None], tile_values[None], jnp.zeros_like(tile_values[None]))
    terms = jnp.einsum(
        "hcsij,hif->cjf", masked, block_scaled_grad, preferred_element_type=jnp.float32
    )

    arrived = lax.all_to_all(terms.astype(jnp.bfloat16), "grp", 0, 0, tiled=True)
    pulled = arrived.astype(jnp.float32).sum(0)

    input_grad = inverse * lax.dot_general(
        pulled, weight.astype(jnp.float32), (((1,), (1,)), ((), ())), precision=HIGHEST,
        preferred_element_type=jnp.float32,
    )
    weight_local = lax.dot_general(
        scaled.astype(jnp.float32), pulled, (((0,), (0,)), ((), ())), precision=HIGHEST,
        preferred_element_type=jnp.float32,
    )
    weight_grad = all_reduce_a2a(weight_local, ("grp", "rep"))
    return (input_grad, weight_grad)


def solution(mesh):
    return jax.shard_map(
        per_device,
        mesh=mesh,
        in_specs=(
            P(("grp", "rep"), None),
            P(),
            P(("grp", "rep"), None),
            P(("grp", "rep"), None),
            P(("grp", "rep")),
            P(("grp", "rep"), None, None, None),
            P(("grp", "rep"), None),
        ),
        out_specs=(P(("grp", "rep"), None), P()),
        check_vma=False,
    )
```

```python
import jax
import jax.numpy as jnp
from jax import lax
from jax.sharding import PartitionSpec as P

HIGHEST = lax.Precision.HIGHEST


def all_reduce_a2a(w, axes):
    count = 1
    for name in axes:
        count *= lax.axis_size(name)
    chunks = w.reshape(count, w.shape[0] // count, w.shape[1])
    owned = lax.all_to_all(chunks, axes, 0, 0, tiled=True).sum(0)
    spread = jnp.broadcast_to(owned[None], chunks.shape)
    return lax.all_to_all(spread, axes, 0, 0, tiled=True).reshape(w.shape)


def per_device(features, weight, preact, grad_out, degree, tile_values, tile_rows):
    rows_here, width = features.shape
    col_tiles, slots, edge, _ = tile_values.shape
    reps = lax.axis_size("rep")
    row_tiles = reps * rows_here // edge
    inverse = lax.rsqrt(degree.astype(jnp.float32))[:, None]
    grad_pre = jnp.where(preact > 0, grad_out, jnp.zeros_like(grad_out))
    scaled = (features.astype(jnp.float32) * inverse).astype(jnp.bfloat16)

    degree_row = jnp.zeros((16, width), jnp.bfloat16).at[0, :rows_here].set(
        degree.astype(jnp.bfloat16)
    )
    packed = jnp.concatenate([grad_pre, degree_row], axis=0)
    me = lax.axis_index("rep")
    parts = [packed]
    for shift in range(1, reps):
        parts.append(lax.ppermute(packed, "rep", [((i + shift) % reps, i) for i in range(reps)]))
    block = jnp.stack(parts)
    block_grad = block[:, :rows_here].reshape(reps * rows_here, width)
    block_degree = block[:, rows_here, :rows_here].reshape(reps * rows_here, 1)
    block_inverse = lax.rsqrt(block_degree.astype(jnp.float32))
    block_scaled_grad = (block_grad.astype(jnp.float32) * block_inverse).astype(jnp.bfloat16)
    block_scaled_grad = block_scaled_grad.reshape(row_tiles, edge, width)

    arrival = jnp.where(tile_rows >= 0, (tile_rows - me + reps) % reps, -1)
    hit = arrival[None] == jnp.arange(row_tiles, dtype=jnp.int32)[:, None, None]
    masked = jnp.where(hit[..., None, None], tile_values[None], jnp.zeros_like(tile_values[None]))
    terms = jnp.einsum(
        "hcsij,hif->cjf", masked, block_scaled_grad, preferred_element_type=jnp.float32
    )

    arrived = lax.all_to_all(terms.astype(jnp.bfloat16), "grp", 0, 0, tiled=True)
    pulled = arrived.astype(jnp.float32).sum(0)

    input_grad = inverse * lax.dot_general(
        pulled, weight.astype(jnp.float32), (((1,), (1,)), ((), ())), precision=HIGHEST,
        preferred_element_type=jnp.float32,
    )
    weight_local = lax.dot_general(
        scaled.astype(jnp.float32), pulled, (((0,), (0,)), ((), ())), precision=HIGHEST,
        preferred_element_type=jnp.float32,
    )
    weight_grad = all_reduce_a2a(weight_local, ("grp", "rep"))
    return (input_grad, weight_grad)


def solution(mesh):
    return jax.shard_map(
        per_device,
        mesh=mesh,
        in_specs=(
            P(("grp", "rep"), None),
            P(),
            P(("grp", "rep"), None),
            P(("grp", "rep"), None),
            P(("grp", "rep")),
            P(("grp", "rep"), None, None, None),
            P(("grp", "rep"), None),
        ),
        out_specs=(P(("grp", "rep"), None), P()),
        check_vma=False,
    )
```

```python
import jax
import jax.numpy as jnp
from jax import lax
from jax.sharding import PartitionSpec as P

HIGHEST = lax.Precision.HIGHEST


def all_reduce_a2a(w, axes):
    count = 1
    for name in axes:
        count *= lax.axis_size(name)
    chunks = w.reshape(count, w.shape[0] // count, w.shape[1])
    owned = lax.all_to_all(chunks, axes, 0, 0, tiled=True).sum(0)
    spread = jnp.broadcast_to(owned[None], chunks.shape)
    return lax.all_to_all(spread, axes, 0, 0, tiled=True).reshape(w.shape)


def per_device(features, weight, preact, grad_out, degree, tile_values, tile_rows):
    rows_here, width = features.shape
    col_tiles, slots, edge, _ = tile_values.shape
    reps = lax.axis_size("rep")
    row_tiles = reps * rows_here // edge
    inverse = lax.rsqrt(degree.astype(jnp.float32))[:, None]
    grad_pre = jnp.where(preact > 0, grad_out, jnp.zeros_like(grad_out))
    scaled = (features.astype(jnp.float32) * inverse).astype(jnp.bfloat16)

    scaled_grad = (grad_pre.astype(jnp.float32) * inverse).astype(jnp.bfloat16)
    me = lax.axis_index("rep")
    parts = [scaled_grad]
    for shift in range(1, reps):
        parts.append(lax.ppermute(scaled_grad, "rep", [((i + shift) % reps, i) for i in range(reps)]))
    block_scaled_grad = jnp.stack(parts)
    block_scaled_grad = block_scaled_grad.reshape(row_tiles, edge, width)

    arrival = jnp.where(tile_rows >= 0, (tile_rows - me + reps) % reps, -1)
    hit = arrival[None] == jnp.arange(row_tiles, dtype=jnp.int32)[:, None, None]
    masked = jnp.where(hit[..., None, None], tile_values[None], jnp.zeros_like(tile_values[None]))
    terms = jnp.einsum(
        "hcsij,hif->cjf", masked, block_scaled_grad, preferred_element_type=jnp.float32
    )

    arrived = lax.all_to_all(terms.astype(jnp.bfloat16), "grp", 0, 0, tiled=True)
    pulled = arrived.astype(jnp.float32).sum(0)

    input_grad = inverse * lax.dot_general(
        pulled, weight.astype(jnp.float32), (((1,), (1,)), ((), ())), precision=HIGHEST,
        preferred_element_type=jnp.float32,
    )
    weight_local = lax.dot_general(
        scaled.astype(jnp.float32), pulled, (((0,), (0,)), ((), ())), precision=HIGHEST,
        preferred_element_type=jnp.float32,
    )
    weight_grad = all_reduce_a2a(weight_local, ("grp", "rep"))
    return (input_grad, weight_grad)


def solution(mesh):
    return jax.shard_map(
        per_device,
        mesh=mesh,
        in_specs=(
            P(("grp", "rep"), None),
            P(),
            P(("grp", "rep"), None),
            P(("grp", "rep"), None),
            P(("grp", "rep")),
            P(("grp", "rep"), None, None, None),
            P(("grp", "rep"), None),
        ),
        out_specs=(P(("grp", "rep"), None), P()),
        check_vma=False,
    )
```

```python
import jax
import jax.numpy as jnp
from jax import lax
from jax.experimental import pallas as pl
from jax.experimental.pallas import tpu as pltpu
from jax.sharding import PartitionSpec as P

HIGHEST = lax.Precision.HIGHEST


def all_reduce_a2a(w, axes):
    count = 1
    for name in axes:
        count *= lax.axis_size(name)
    chunks = w.reshape(count, w.shape[0] // count, w.shape[1])
    owned = lax.all_to_all(chunks, axes, 0, 0, tiled=True).sum(0)
    spread = jnp.broadcast_to(owned[None], chunks.shape)
    return lax.all_to_all(spread, axes, 0, 0, tiled=True).reshape(w.shape)


def transposed_terms(arrival, tile_values, block):
    col_tiles, slots, edge, _ = tile_values.shape
    row_tiles, _, width = block.shape
    per_step = min(col_tiles, 8)

    def kernel(rows_ref, tiles_ref, block_ref, out_ref):
        step = pl.program_id(0)
        for c in range(per_step):
            acc = jnp.zeros((edge, width), jnp.float32)
            for s in range(slots):
                row = rows_ref[(step * per_step + c) * slots + s]
                picked = block_ref[jnp.clip(row, 0, row_tiles - 1)]
                contrib = lax.dot_general(
                    tiles_ref[c, s], picked, (((0,), (0,)), ((), ())),
                    preferred_element_type=jnp.float32,
                )
                acc = acc + jnp.where(row >= 0, contrib, jnp.zeros_like(contrib))
            out_ref[c] = acc.astype(out_ref.dtype)

    grid_spec = pltpu.PrefetchScalarGridSpec(
        num_scalar_prefetch=1,
        grid=(col_tiles // per_step,),
        in_specs=[
            pl.BlockSpec((per_step, slots, edge, edge), lambda b, rows: (b, 0, 0, 0)),
            pl.BlockSpec((row_tiles, edge, width), lambda b, rows: (0, 0, 0)),
        ],
        out_specs=pl.BlockSpec((per_step, edge, width), lambda b, rows: (b, 0, 0)),
    )
    return pl.pallas_call(
        kernel,
        out_shape=jax.ShapeDtypeStruct((col_tiles, edge, width), jnp.bfloat16),
        grid_spec=grid_spec,
        cost_estimate=pl.CostEstimate(
            flops=2 * col_tiles * slots * edge * edge * width,
            transcendentals=0,
            bytes_accessed=2 * (tile_values.size + block.size + col_tiles * edge * width),
        ),
    )(arrival.reshape(-1), tile_values, block)


def per_device(features, weight, preact, grad_out, degree, tile_values, tile_rows):
    rows_here, width = features.shape
    col_tiles, slots, edge, _ = tile_values.shape
    reps = lax.axis_size("rep")
    row_tiles = reps * rows_here // edge
    inverse = lax.rsqrt(degree.astype(jnp.float32))[:, None]
    grad_pre = jnp.where(preact > 0, grad_out, jnp.zeros_like(grad_out))
    scaled = (features.astype(jnp.float32) * inverse).astype(jnp.bfloat16)

    scaled_grad = (grad_pre.astype(jnp.float32) * inverse).astype(jnp.bfloat16)
    me = lax.axis_index("rep")
    parts = [scaled_grad]
    for shift in range(1, reps):
        parts.append(lax.ppermute(scaled_grad, "rep", [((i + shift) % reps, i) for i in range(reps)]))
    block_scaled_grad = jnp.stack(parts)
    block_scaled_grad = block_scaled_grad.reshape(row_tiles, edge, width)

    arrival = jnp.where(tile_rows >= 0, (tile_rows - me + reps) % reps, -1)
    terms = transposed_terms(arrival, tile_values, block_scaled_grad)

    arrived = lax.all_to_all(terms, "grp", 0, 0, tiled=True)
    pulled = arrived.astype(jnp.float32).sum(0)

    input_grad = inverse * lax.dot_general(
        pulled, weight.astype(jnp.float32), (((1,), (1,)), ((), ())), precision=HIGHEST,
        preferred_element_type=jnp.float32,
    )
    weight_local = lax.dot_general(
        scaled.astype(jnp.float32), pulled, (((0,), (0,)), ((), ())), precision=HIGHEST,
        preferred_element_type=jnp.float32,
    )
    weight_grad = all_reduce_a2a(weight_local, ("grp", "rep"))
    return (input_grad, weight_grad)


def solution(mesh):
    return jax.shard_map(
        per_device,
        mesh=mesh,
        in_specs=(
            P(("grp", "rep"), None),
            P(),
            P(("grp", "rep"), None),
            P(("grp", "rep"), None),
            P(("grp", "rep")),
            P(("grp", "rep"), None, None, None),
            P(("grp", "rep"), None),
        ),
        out_specs=(P(("grp", "rep"), None), P()),
        check_vma=False,
    )
```

```python
import jax
import jax.numpy as jnp
from jax import lax
from jax.experimental import pallas as pl
from jax.experimental.pallas import tpu as pltpu
from jax.sharding import PartitionSpec as P

HIGHEST = lax.Precision.HIGHEST


def all_reduce_a2a(w, axes):
    count = 1
    for name in axes:
        count *= lax.axis_size(name)
    chunks = w.reshape(count, w.shape[0] // count, w.shape[1])
    owned = lax.all_to_all(chunks, axes, 0, 0, tiled=True).sum(0)
    spread = jnp.broadcast_to(owned[None], chunks.shape)
    return lax.all_to_all(spread, axes, 0, 0, tiled=True).reshape(w.shape)


def transposed_terms(tile_rows, tile_values, block_t):
    col_tiles, slots, edge, _ = tile_values.shape
    kinds, width, _ = block_t.shape
    reps = kinds - 1
    per_step = min(col_tiles, 4)

    def kernel(rows_ref, tiles_ref, block_ref, out_ref):
        step = pl.program_id(0)
        me = lax.axis_index("rep")
        for c in range(per_step):
            acc = jnp.zeros((width, edge), jnp.float32)
            for s in range(slots):
                row = rows_ref[step * per_step + c, s]
                k = jnp.where(row >= 0, (row - me + reps) % reps, reps)
                acc = acc + jnp.dot(
                    block_ref[k], tiles_ref[c, s], preferred_element_type=jnp.float32
                )
            out_ref[c] = acc.astype(out_ref.dtype)

    grid_spec = pltpu.PrefetchScalarGridSpec(
        num_scalar_prefetch=1,
        grid=(col_tiles // per_step,),
        in_specs=[
            pl.BlockSpec((per_step, slots, edge, edge), lambda b, rows: (b, 0, 0, 0)),
            pl.BlockSpec((kinds, width, edge), lambda b, rows: (0, 0, 0)),
        ],
        out_specs=pl.BlockSpec((per_step, width, edge), lambda b, rows: (b, 0, 0)),
    )
    return pl.pallas_call(
        kernel,
        out_shape=jax.ShapeDtypeStruct((col_tiles, width, edge), jnp.bfloat16),
        grid_spec=grid_spec,
        cost_estimate=pl.CostEstimate(
            flops=2 * col_tiles * slots * edge * edge * width,
            transcendentals=0,
            bytes_accessed=2 * (tile_values.size + block_t.size + col_tiles * edge * width),
        ),
    )(tile_rows, tile_values, block_t)


def per_device(features, weight, preact, grad_out, degree, tile_values, tile_rows):
    rows_here, width = features.shape
    col_tiles, slots, edge, _ = tile_values.shape
    reps = lax.axis_size("rep")
    row_tiles = reps * rows_here // edge
    inverse = lax.rsqrt(degree.astype(jnp.float32))[:, None]
    grad_pre = jnp.where(preact > 0, grad_out, jnp.zeros_like(grad_out))
    scaled = (features.astype(jnp.float32) * inverse).astype(jnp.bfloat16)

    scaled_grad_t = (grad_pre.astype(jnp.float32) * inverse).astype(jnp.bfloat16).T
    parts = [scaled_grad_t]
    for shift in range(1, reps):
        parts.append(lax.ppermute(scaled_grad_t, "rep", [((i + shift) % reps, i) for i in range(reps)]))
    parts.append(jnp.zeros_like(scaled_grad_t))
    block_t = jnp.stack(parts)
    terms_t = transposed_terms(tile_rows, tile_values, block_t)

    arrived = lax.all_to_all(terms_t, "grp", 0, 0, tiled=True)
    pulled_t = arrived.astype(jnp.float32).sum(0)

    input_grad = inverse * lax.dot_general(
        pulled_t, weight.astype(jnp.float32), (((0,), (1,)), ((), ())), precision=HIGHEST,
        preferred_element_type=jnp.float32,
    )
    weight_local = lax.dot_general(
        scaled.astype(jnp.float32), pulled_t, (((0,), (1,)), ((), ())), precision=HIGHEST,
        preferred_element_type=jnp.float32,
    )
    weight_grad = all_reduce_a2a(weight_local, ("grp", "rep"))
    return (input_grad, weight_grad)


def solution(mesh):
    return jax.shard_map(
        per_device,
        mesh=mesh,
        in_specs=(
            P(("grp", "rep"), None),
            P(),
            P(("grp", "rep"), None),
            P(("grp", "rep"), None),
            P(("grp", "rep")),
            P(("grp", "rep"), None, None, None),
            P(("grp", "rep"), None),
        ),
        out_specs=(P(("grp", "rep"), None), P()),
        check_vma=False,
    )
```

```python
import jax
import jax.numpy as jnp
from jax import lax
from jax.sharding import PartitionSpec as P

HIGHEST = lax.Precision.HIGHEST


def all_reduce_a2a(w, axes):
    count = 1
    for name in axes:
        count *= lax.axis_size(name)
    chunks = w.reshape(count, w.shape[0] // count, w.shape[1])
    owned = lax.all_to_all(chunks, axes, 0, 0, tiled=True).sum(0)
    spread = jnp.broadcast_to(owned[None], chunks.shape)
    return lax.all_to_all(spread, axes, 0, 0, tiled=True).reshape(w.shape)


def per_device(features, weight, preact, grad_out, degree, tile_values, tile_rows):
    rows_here, width = features.shape
    col_tiles, slots, edge, _ = tile_values.shape
    reps = lax.axis_size("rep")
    row_tiles = reps * rows_here // edge
    inverse = lax.rsqrt(degree.astype(jnp.float32))[:, None]
    grad_pre = jnp.where(preact > 0, grad_out, jnp.zeros_like(grad_out))
    scaled = (features.astype(jnp.float32) * inverse).astype(jnp.bfloat16)

    scaled_grad = (grad_pre.astype(jnp.float32) * inverse).astype(jnp.bfloat16)
    me = lax.axis_index("rep")
    parts = [scaled_grad]
    for shift in range(1, reps):
        parts.append(lax.ppermute(scaled_grad, "rep", [((i + shift) % reps, i) for i in range(reps)]))
    block_scaled_grad = jnp.stack(parts)
    block_scaled_grad = block_scaled_grad.reshape(row_tiles, edge, width)

    arrival = jnp.where(tile_rows >= 0, (tile_rows - me + reps) % reps, -1)
    onehot = (arrival[..., None] == jnp.arange(row_tiles, dtype=jnp.int32)).astype(jnp.bfloat16)
    picked = jnp.einsum(
        "csh,hif->csif", onehot, block_scaled_grad, preferred_element_type=jnp.float32
    ).astype(jnp.bfloat16)
    terms = jnp.einsum("csij,csif->cjf", tile_values, picked, preferred_element_type=jnp.float32)

    arrived = lax.all_to_all(terms.astype(jnp.bfloat16), "grp", 0, 0, tiled=True)
    pulled = arrived.astype(jnp.float32).sum(0)

    input_grad = inverse * lax.dot_general(
        pulled, weight.astype(jnp.float32), (((1,), (1,)), ((), ())), precision=HIGHEST,
        preferred_element_type=jnp.float32,
    )
    weight_local = lax.dot_general(
        scaled.astype(jnp.float32), pulled, (((0,), (0,)), ((), ())), precision=HIGHEST,
        preferred_element_type=jnp.float32,
    )
    weight_grad = all_reduce_a2a(weight_local, ("grp", "rep"))
    return (input_grad, weight_grad)


def solution(mesh):
    return jax.shard_map(
        per_device,
        mesh=mesh,
        in_specs=(
            P(("grp", "rep"), None),
            P(),
            P(("grp", "rep"), None),
            P(("grp", "rep"), None),
            P(("grp", "rep")),
            P(("grp", "rep"), None, None, None),
            P(("grp", "rep"), None),
        ),
        out_specs=(P(("grp", "rep"), None), P()),
        check_vma=False,
    )
```

```python
import jax
import jax.numpy as jnp
from jax import lax
from jax.sharding import PartitionSpec as P

HIGHEST = lax.Precision.HIGHEST


def all_reduce_a2a(w, axes, early):
    count = 1
    for name in axes:
        count *= lax.axis_size(name)
    chunks = w.reshape(count, w.shape[0] // count, w.shape[1])
    owned = lax.all_to_all(chunks, axes, 0, 0, tiled=True).sum(0)
    spread = jnp.broadcast_to(owned[None], chunks.shape)
    spread, early = lax.optimization_barrier((spread, early))
    return lax.all_to_all(spread, axes, 0, 0, tiled=True).reshape(w.shape), early


def per_device(features, weight, preact, grad_out, degree, tile_values, tile_rows):
    rows_here, width = features.shape
    col_tiles, slots, edge, _ = tile_values.shape
    reps = lax.axis_size("rep")
    row_tiles = reps * rows_here // edge
    inverse = lax.rsqrt(degree.astype(jnp.float32))[:, None]
    grad_pre = jnp.where(preact > 0, grad_out, jnp.zeros_like(grad_out))
    scaled = (features.astype(jnp.float32) * inverse).astype(jnp.bfloat16)

    scaled_grad = (grad_pre.astype(jnp.float32) * inverse).astype(jnp.bfloat16)
    me = lax.axis_index("rep")
    parts = [scaled_grad]
    for shift in range(1, reps):
        parts.append(lax.ppermute(scaled_grad, "rep", [((i + shift) % reps, i) for i in range(reps)]))
    block_scaled_grad = jnp.stack(parts)
    block_scaled_grad = block_scaled_grad.reshape(row_tiles, edge, width)

    arrival = jnp.where(tile_rows >= 0, (tile_rows - me + reps) % reps, -1)
    hit = arrival[None] == jnp.arange(row_tiles, dtype=jnp.int32)[:, None, None]
    masked = jnp.where(hit[..., None, None], tile_values[None], jnp.zeros_like(tile_values[None]))
    terms = jnp.einsum(
        "hcsij,hif->cjf", masked, block_scaled_grad, preferred_element_type=jnp.float32
    )

    arrived = lax.all_to_all(terms.astype(jnp.bfloat16), "grp", 0, 0, tiled=True)
    pulled = arrived.astype(jnp.float32).sum(0)

    def input_rows(rows):
        return inverse[rows] * lax.dot_general(
            pulled[rows], weight.astype(jnp.float32), (((1,), (1,)), ((), ())), precision=HIGHEST,
            preferred_element_type=jnp.float32,
        )

    half = rows_here // 2
    first_rows = input_rows(slice(0, half))
    weight_local = lax.dot_general(
        scaled.astype(jnp.float32), pulled, (((0,), (0,)), ((), ())), precision=HIGHEST,
        preferred_element_type=jnp.float32,
    )
    weight_grad, first_rows = all_reduce_a2a(weight_local, ("grp", "rep"), first_rows)
    input_grad = jnp.concatenate([first_rows, input_rows(slice(half, rows_here))], axis=0)
    return (input_grad, weight_grad)


def solution(mesh):
    return jax.shard_map(
        per_device,
        mesh=mesh,
        in_specs=(
            P(("grp", "rep"), None),
            P(),
            P(("grp", "rep"), None),
            P(("grp", "rep"), None),
            P(("grp", "rep")),
            P(("grp", "rep"), None, None, None),
            P(("grp", "rep"), None),
        ),
        out_specs=(P(("grp", "rep"), None), P()),
        check_vma=False,
    )
```

```python
import jax
import jax.numpy as jnp
from jax import lax
from jax.sharding import PartitionSpec as P

HIGHEST = lax.Precision.HIGHEST


def all_reduce_a2a(w, axes):
    count = 1
    for name in axes:
        count *= lax.axis_size(name)
    chunks = w.reshape(count, w.shape[0] // count, w.shape[1])
    owned = lax.all_to_all(chunks, axes, 0, 0, tiled=True).sum(0)
    spread = jnp.broadcast_to(owned[None], chunks.shape)
    return lax.all_to_all(spread, axes, 0, 0, tiled=True).reshape(w.shape)


def per_device(features, weight, preact, grad_out, degree, tile_values, tile_rows):
    rows_here, width = features.shape
    col_tiles, slots, edge, _ = tile_values.shape
    reps = lax.axis_size("rep")
    row_tiles = reps * rows_here // edge
    inverse = lax.rsqrt(degree.astype(jnp.float32))[:, None]
    grad_pre = jnp.where(preact > 0, grad_out, jnp.zeros_like(grad_out))
    scaled = (features.astype(jnp.float32) * inverse).astype(jnp.bfloat16)

    scaled_grad = (grad_pre.astype(jnp.float32) * inverse).astype(jnp.bfloat16)
    me = lax.axis_index("rep")
    parts = [scaled_grad]
    for shift in range(1, reps):
        parts.append(lax.ppermute(scaled_grad, "rep", [((i + shift) % reps, i) for i in range(reps)]))
    arrived_rows = jnp.stack(parts[1:])

    arrival = jnp.where(tile_rows >= 0, (tile_rows - me + reps) % reps, -1)
    hit = arrival[None] == jnp.arange(reps, dtype=jnp.int32)[:, None, None]
    masked = jnp.where(hit[..., None, None], tile_values[None], jnp.zeros_like(tile_values[None]))
    own_terms = jnp.einsum(
        "csij,if->cjf", masked[0], scaled_grad, preferred_element_type=jnp.float32
    )
    terms = own_terms + jnp.einsum(
        "hcsij,hif->cjf", masked[1:], arrived_rows, preferred_element_type=jnp.float32
    )

    arrived = lax.all_to_all(terms.astype(jnp.bfloat16), "grp", 0, 0, tiled=True)
    pulled = arrived.astype(jnp.float32).sum(0)

    input_grad = inverse * lax.dot_general(
        pulled, weight.astype(jnp.float32), (((1,), (1,)), ((), ())), precision=HIGHEST,
        preferred_element_type=jnp.float32,
    )
    weight_local = lax.dot_general(
        scaled.astype(jnp.float32), pulled, (((0,), (0,)), ((), ())), precision=HIGHEST,
        preferred_element_type=jnp.float32,
    )
    weight_grad = all_reduce_a2a(weight_local, ("grp", "rep"))
    return (input_grad, weight_grad)


def solution(mesh):
    return jax.shard_map(
        per_device,
        mesh=mesh,
        in_specs=(
            P(("grp", "rep"), None),
            P(),
            P(("grp", "rep"), None),
            P(("grp", "rep"), None),
            P(("grp", "rep")),
            P(("grp", "rep"), None, None, None),
            P(("grp", "rep"), None),
        ),
        out_specs=(P(("grp", "rep"), None), P()),
        check_vma=False,
    )
```

```python
import jax
import jax.numpy as jnp
from jax import lax
from jax.sharding import PartitionSpec as P

HIGHEST = lax.Precision.HIGHEST


def all_reduce_a2a(w, axes):
    count = 1
    for name in axes:
        count *= lax.axis_size(name)
    chunks = w.reshape(count, w.shape[0] // count, w.shape[1])
    owned = lax.all_to_all(chunks, axes, 0, 0, tiled=True).sum(0)
    spread = jnp.broadcast_to(owned[None], chunks.shape)
    return lax.all_to_all(spread, axes, 0, 0, tiled=True).reshape(w.shape)


def per_device(features, weight, preact, grad_out, degree, tile_values, tile_rows):
    rows_here, width = features.shape
    col_tiles, slots, edge, _ = tile_values.shape
    reps = lax.axis_size("rep")
    row_tiles = reps * rows_here // edge
    inverse = lax.rsqrt(degree.astype(jnp.float32))[:, None]
    grad_pre = jnp.where(preact > 0, grad_out, jnp.zeros_like(grad_out))
    scaled = (features.astype(jnp.float32) * inverse).astype(jnp.bfloat16)

    scaled_grad = (grad_pre.astype(jnp.float32) * inverse).astype(jnp.bfloat16)
    me = lax.axis_index("rep")
    parts = [scaled_grad]
    for shift in range(1, reps):
        parts.append(lax.ppermute(scaled_grad, "rep", [((i + shift) % reps, i) for i in range(reps)]))
    block_scaled_grad = jnp.stack(parts)
    block_scaled_grad = block_scaled_grad.reshape(row_tiles, edge, width)

    arrival = jnp.where(tile_rows >= 0, (tile_rows - me + reps) % reps, -1)
    hit = arrival[None] == jnp.arange(row_tiles, dtype=jnp.int32)[:, None, None]
    tiles = tile_values[None].astype(jnp.float32)
    summed = jnp.where(hit[..., None, None], tiles, jnp.zeros_like(tiles)).sum(axis=2)
    high = summed.astype(jnp.bfloat16)
    low = (summed - high.astype(jnp.float32)).astype(jnp.bfloat16)
    terms = jnp.einsum(
        "phcij,hif->cjf", jnp.stack([high, low]), block_scaled_grad,
        preferred_element_type=jnp.float32,
    )

    arrived = lax.all_to_all(terms.astype(jnp.bfloat16), "grp", 0, 0, tiled=True)
    pulled = arrived.astype(jnp.float32).sum(0)

    input_grad = inverse * lax.dot_general(
        pulled, weight.astype(jnp.float32), (((1,), (1,)), ((), ())), precision=HIGHEST,
        preferred_element_type=jnp.float32,
    )
    weight_local = lax.dot_general(
        scaled.astype(jnp.float32), pulled, (((0,), (0,)), ((), ())), precision=HIGHEST,
        preferred_element_type=jnp.float32,
    )
    weight_grad = all_reduce_a2a(weight_local, ("grp", "rep"))
    return (input_grad, weight_grad)


def solution(mesh):
    return jax.shard_map(
        per_device,
        mesh=mesh,
        in_specs=(
            P(("grp", "rep"), None),
            P(),
            P(("grp", "rep"), None),
            P(("grp", "rep"), None),
            P(("grp", "rep")),
            P(("grp", "rep"), None, None, None),
            P(("grp", "rep"), None),
        ),
        out_specs=(P(("grp", "rep"), None), P()),
        check_vma=False,
    )
```

```python
import jax
import jax.numpy as jnp
from jax import lax
from jax.sharding import PartitionSpec as P

HIGHEST = lax.Precision.HIGHEST


def all_reduce_a2a(w, axes):
    count = 1
    for name in axes:
        count *= lax.axis_size(name)
    chunks = w.reshape(count, w.shape[0] // count, w.shape[1])
    owned = lax.all_to_all(chunks, axes, 0, 0, tiled=True).sum(0)
    spread = jnp.broadcast_to(owned[None], chunks.shape)
    return lax.all_to_all(spread, axes, 0, 0, tiled=True).reshape(w.shape)


def per_device(features, weight, preact, grad_out, degree, tile_values, tile_rows):
    rows_here, width = features.shape
    col_tiles, slots, edge, _ = tile_values.shape
    reps = lax.axis_size("rep")
    row_tiles = reps * rows_here // edge
    inverse = lax.rsqrt(degree.astype(jnp.float32))[:, None]
    grad_pre = jnp.where(preact > 0, grad_out, jnp.zeros_like(grad_out))

    scaled_grad = (grad_pre.astype(jnp.float32) * inverse).astype(jnp.bfloat16)
    me = lax.axis_index("rep")
    parts = [scaled_grad]
    for shift in range(1, reps):
        parts.append(lax.ppermute(scaled_grad, "rep", [((i + shift) % reps, i) for i in range(reps)]))
    block_scaled_grad = jnp.stack(parts)
    block_scaled_grad = block_scaled_grad.reshape(row_tiles, edge, width)

    arrival = jnp.where(tile_rows >= 0, (tile_rows - me + reps) % reps, -1)
    hit = arrival[None] == jnp.arange(row_tiles, dtype=jnp.int32)[:, None, None]
    masked = jnp.where(hit[..., None, None], tile_values[None], jnp.zeros_like(tile_values[None]))
    terms = jnp.einsum(
        "hcsij,hif->cjf", masked, block_scaled_grad, preferred_element_type=jnp.float32
    )

    arrived = lax.all_to_all(terms.astype(jnp.bfloat16), "grp", 0, 0, tiled=True)
    pulled = arrived.astype(jnp.float32).sum(0)

    input_grad = inverse * lax.dot_general(
        pulled, weight.astype(jnp.float32), (((1,), (1,)), ((), ())), precision=HIGHEST,
        preferred_element_type=jnp.float32,
    )
    late_features, pulled = lax.optimization_barrier((features, pulled))
    scaled = (late_features.astype(jnp.float32) * inverse).astype(jnp.bfloat16)
    weight_local = lax.dot_general(
        scaled.astype(jnp.float32), pulled, (((0,), (0,)), ((), ())), precision=HIGHEST,
        preferred_element_type=jnp.float32,
    )
    weight_grad = all_reduce_a2a(weight_local, ("grp", "rep"))
    return (input_grad, weight_grad)


def solution(mesh):
    return jax.shard_map(
        per_device,
        mesh=mesh,
        in_specs=(
            P(("grp", "rep"), None),
            P(),
            P(("grp", "rep"), None),
            P(("grp", "rep"), None),
            P(("grp", "rep")),
            P(("grp", "rep"), None, None, None),
            P(("grp", "rep"), None),
        ),
        out_specs=(P(("grp", "rep"), None), P()),
        check_vma=False,
    )
```

```python
import jax
import jax.numpy as jnp
from jax import lax
from jax.sharding import PartitionSpec as P

HIGHEST = lax.Precision.HIGHEST


def all_reduce_a2a(w, axes):
    count = 1
    for name in axes:
        count *= lax.axis_size(name)
    chunks = w.reshape(count, w.shape[0] // count, w.shape[1])
    owned = lax.all_to_all(chunks, axes, 0, 0, tiled=True).sum(0)
    spread = jnp.broadcast_to(owned[None], chunks.shape)
    return lax.all_to_all(spread, axes, 0, 0, tiled=True).reshape(w.shape)


def per_device(features, weight, preact, grad_out, degree, tile_values, tile_rows):
    rows_here, width = features.shape
    col_tiles, slots, edge, _ = tile_values.shape
    reps = lax.axis_size("rep")
    row_tiles = reps * rows_here // edge
    inverse = lax.rsqrt(degree.astype(jnp.float32))[:, None]
    grad_pre = jnp.where(preact > 0, grad_out, jnp.zeros_like(grad_out))

    scaled_grad = (grad_pre.astype(jnp.float32) * inverse).astype(jnp.bfloat16)
    me = lax.axis_index("rep")
    parts = [scaled_grad]
    for shift in range(1, reps):
        parts.append(lax.ppermute(scaled_grad, "rep", [((i + shift) % reps, i) for i in range(reps)]))
    block_scaled_grad = jnp.stack(parts)
    block_scaled_grad = block_scaled_grad.reshape(row_tiles, edge, width)

    arrival = jnp.where(tile_rows >= 0, (tile_rows - me + reps) % reps, -1)
    hit = arrival[None] == jnp.arange(row_tiles, dtype=jnp.int32)[:, None, None]
    masked = jnp.where(hit[..., None, None], tile_values[None], jnp.zeros_like(tile_values[None]))
    terms = jnp.einsum(
        "hcsij,hif->cjf", masked, block_scaled_grad, preferred_element_type=jnp.float32
    )

    arrived = lax.all_to_all(terms.astype(jnp.bfloat16), "grp", 0, 0, tiled=True)
    pulled = arrived.astype(jnp.float32).sum(0)

    input_grad = inverse * lax.dot_general(
        pulled, weight.astype(jnp.float32), (((1,), (1,)), ((), ())), precision=HIGHEST,
        preferred_element_type=jnp.float32,
    )
    late_features, pulled = lax.optimization_barrier((features, pulled))
    scaled = (late_features.astype(jnp.float32) * inverse).astype(jnp.bfloat16)
    pulled_high = pulled.astype(jnp.bfloat16)
    pulled_low = (pulled - pulled_high.astype(jnp.float32)).astype(jnp.bfloat16)
    weight_local = sum(
        lax.dot_general(
            scaled, part, (((0,), (0,)), ((), ())), preferred_element_type=jnp.float32
        )
        for part in (pulled_high, pulled_low)
    )
    weight_grad = all_reduce_a2a(weight_local, ("grp", "rep"))
    return (input_grad, weight_grad)


def solution(mesh):
    return jax.shard_map(
        per_device,
        mesh=mesh,
        in_specs=(
            P(("grp", "rep"), None),
            P(),
            P(("grp", "rep"), None),
            P(("grp", "rep"), None),
            P(("grp", "rep")),
            P(("grp", "rep"), None, None, None),
            P(("grp", "rep"), None),
        ),
        out_specs=(P(("grp", "rep"), None), P()),
        check_vma=False,
    )
```

```python
import jax
import jax.numpy as jnp
from jax import lax
from jax.sharding import PartitionSpec as P

HIGHEST = lax.Precision.HIGHEST


def all_reduce_a2a(w, axes):
    count = 1
    for name in axes:
        count *= lax.axis_size(name)
    chunks = w.reshape(count, w.shape[0] // count, w.shape[1])
    owned = lax.all_to_all(chunks, axes, 0, 0, tiled=True).sum(0)
    spread = jnp.broadcast_to(owned[None], chunks.shape)
    return lax.all_to_all(spread, axes, 0, 0, tiled=True).reshape(w.shape)


def per_device(features, weight, preact, grad_out, degree, tile_values, tile_rows):
    rows_here, width = features.shape
    col_tiles, slots, edge, _ = tile_values.shape
    reps = lax.axis_size("rep")
    row_tiles = reps * rows_here // edge
    inverse = lax.rsqrt(degree.astype(jnp.float32))[:, None]
    grad_pre = jnp.where(preact > 0, grad_out, jnp.zeros_like(grad_out))

    scaled_grad = (grad_pre.astype(jnp.float32) * inverse).astype(jnp.bfloat16)
    me = lax.axis_index("rep")
    parts = [scaled_grad]
    for shift in range(1, reps):
        parts.append(lax.ppermute(scaled_grad, "rep", [((i + shift) % reps, i) for i in range(reps)]))
    block_scaled_grad = jnp.stack(parts)
    block_scaled_grad = block_scaled_grad.reshape(row_tiles, edge, width)

    arrival = jnp.where(tile_rows >= 0, (tile_rows - me + reps) % reps, -1)
    hit = arrival[None] == jnp.arange(row_tiles, dtype=jnp.int32)[:, None, None]
    masked = jnp.where(hit[..., None, None], tile_values[None], jnp.zeros_like(tile_values[None]))
    terms = jnp.einsum(
        "hcsij,hif->cjf", masked, block_scaled_grad, preferred_element_type=jnp.float32
    )

    late_features, terms = lax.optimization_barrier((features, terms))
    scaled = (late_features.astype(jnp.float32) * inverse).astype(jnp.bfloat16)

    arrived = lax.all_to_all(terms.astype(jnp.bfloat16), "grp", 0, 0, tiled=True)
    pulled = arrived.astype(jnp.float32).sum(0)

    input_grad = inverse * lax.dot_general(
        pulled, weight.astype(jnp.float32), (((1,), (1,)), ((), ())), precision=HIGHEST,
        preferred_element_type=jnp.float32,
    )
    weight_local = lax.dot_general(
        scaled.astype(jnp.float32), pulled, (((0,), (0,)), ((), ())), precision=HIGHEST,
        preferred_element_type=jnp.float32,
    )
    weight_grad = all_reduce_a2a(weight_local, ("grp", "rep"))
    return (input_grad, weight_grad)


def solution(mesh):
    return jax.shard_map(
        per_device,
        mesh=mesh,
        in_specs=(
            P(("grp", "rep"), None),
            P(),
            P(("grp", "rep"), None),
            P(("grp", "rep"), None),
            P(("grp", "rep")),
            P(("grp", "rep"), None, None, None),
            P(("grp", "rep"), None),
        ),
        out_specs=(P(("grp", "rep"), None), P()),
        check_vma=False,
    )
```

```python
import jax
import jax.numpy as jnp
from jax import lax
from jax.sharding import PartitionSpec as P

HIGHEST = lax.Precision.HIGHEST


def all_reduce_a2a(w, axes, early):
    count = 1
    for name in axes:
        count *= lax.axis_size(name)
    chunks = w.reshape(count, w.shape[0] // count, w.shape[1])
    owned = lax.all_to_all(chunks, axes, 0, 0, tiled=True).sum(0)
    spread = jnp.broadcast_to(owned[None], chunks.shape)
    spread, early = lax.optimization_barrier((spread, early))
    return lax.all_to_all(spread, axes, 0, 0, tiled=True).reshape(w.shape), early


def per_device(features, weight, preact, grad_out, degree, tile_values, tile_rows):
    rows_here, width = features.shape
    col_tiles, slots, edge, _ = tile_values.shape
    reps = lax.axis_size("rep")
    row_tiles = reps * rows_here // edge
    inverse = lax.rsqrt(degree.astype(jnp.float32))[:, None]
    grad_pre = jnp.where(preact > 0, grad_out, jnp.zeros_like(grad_out))

    scaled_grad = (grad_pre.astype(jnp.float32) * inverse).astype(jnp.bfloat16)
    me = lax.axis_index("rep")
    parts = [scaled_grad]
    for shift in range(1, reps):
        parts.append(lax.ppermute(scaled_grad, "rep", [((i + shift) % reps, i) for i in range(reps)]))
    block_scaled_grad = jnp.stack(parts)
    block_scaled_grad = block_scaled_grad.reshape(row_tiles, edge, width)

    arrival = jnp.where(tile_rows >= 0, (tile_rows - me + reps) % reps, -1)
    hit = arrival[None] == jnp.arange(row_tiles, dtype=jnp.int32)[:, None, None]
    masked = jnp.where(hit[..., None, None], tile_values[None], jnp.zeros_like(tile_values[None]))
    terms = jnp.einsum(
        "hcsij,hif->cjf", masked, block_scaled_grad, preferred_element_type=jnp.float32
    )

    arrived = lax.all_to_all(terms.astype(jnp.bfloat16), "grp", 0, 0, tiled=True)
    pulled = arrived.astype(jnp.float32).sum(0)

    def projected_part(cols):
        return lax.dot_general(
            pulled[:, cols], weight[:, cols].astype(jnp.float32), (((1,), (1,)), ((), ())),
            precision=HIGHEST, preferred_element_type=jnp.float32,
        )

    half = width // 2
    first_part = projected_part(slice(0, half))
    late_features, pulled = lax.optimization_barrier((features, pulled))
    scaled = (late_features.astype(jnp.float32) * inverse).astype(jnp.bfloat16)
    weight_local = lax.dot_general(
        scaled.astype(jnp.float32), pulled, (((0,), (0,)), ((), ())), precision=HIGHEST,
        preferred_element_type=jnp.float32,
    )
    weight_grad, first_part = all_reduce_a2a(weight_local, ("grp", "rep"), first_part)
    input_grad = inverse * (first_part + projected_part(slice(half, width)))
    return (input_grad, weight_grad)


def solution(mesh):
    return jax.shard_map(
        per_device,
        mesh=mesh,
        in_specs=(
            P(("grp", "rep"), None),
            P(),
            P(("grp", "rep"), None),
            P(("grp", "rep"), None),
            P(("grp", "rep")),
            P(("grp", "rep"), None, None, None),
            P(("grp", "rep"), None),
        ),
        out_specs=(P(("grp", "rep"), None), P()),
        check_vma=False,
    )
```
